128 devices in a mesh: mp: 8 (over z_hi, y), layer: 4 (over x), example: 4 (over z_lo, core).
Axes of the slice: x: 4, y: 4, z: 4 (z_hi: 2, z_lo: 2; z = z_hi * 2 + z_lo), core: 2. Of those that a mesh axis runs over, the one named last changes fastest.
Arguments:
- cotangent: bfloat16 [4, 2048, 8192], P(None, ('mp', 'layer', 'example')), may hold values from -6 to 6
- down_weight: bfloat16 [4, 14336, 8192], P('layer', 'mp', 'example'), may hold values from -0.0625 to 0.0625
- gate_act: bfloat16 [4, 2048, 14336], P('layer', None, 'mp'), may hold values from -0.25 to 2.5
- layer_input: bfloat16 [4, 2048, 8192], P('layer', ('mp', 'example')), may hold values from -6 to 6
- proj_out: bfloat16 [4, 64, 14336], P('layer', None, 'mp'), may hold values from -0.046875 to 0.046875
- proj_in: bfloat16 [4, 64, 8192], P('layer'), may hold values from -0.0625 to 0.0625
- queries: bfloat16 [4, 1024, 4096], P('layer', ('mp', 'example')), may hold values from -0.09375 to 0.09375
- hessian_prior: float32 [4, 4096, 4096], P('layer', ('mp', 'example')), may hold values from -4 to 4
- doc_lengths: int32 [32], P(('mp', 'example')), may hold values from 16 to 64, as said below
Outputs:
- hessian: float32 [4, 4096, 4096], P('layer', ('mp', 'example'))
- scores: float32 [1024, 32], P(('mp', 'example'))
The draws below stay inside these ranges and needn't reach their ends.
Inputs may be any that keep to these rules, and one draw needn't show every extreme that they name: Document n holds doc_lengths[n] real tokens at the start of its 64 positions; the rest is padding.
All inputs are finite; a program needn't handle non-finite values.
Results may differ from the reference program's by a relative error of at most 0.0003.
Values may be sent and summed in bfloat16 or wider, within the bound.
No kernel may reach another device: no remote copies, remote signals or barrier semaphores. Data moves between devices by JAX's collectives and lax.ppermute only.
A program may use at most 128 MiB of HBM per device.

```python
import jax
import jax.numpy as jnp
from jax import lax

D = 8192
FFW = 14336
KO = 64
KI = 64
NQ = 1024
SEQ = 64
LAYERS = 4
DOCS = 32
TOKENS = 2048
KP = 4096


def draw_doc_lengths(key, part):
    lengths = jax.random.randint(key, (DOCS,), SEQ // 4, SEQ + 1)
    positions = jnp.arange(DOCS)
    lengths = jnp.where(positions == 0, SEQ, lengths)
    lengths = jnp.where(positions == DOCS - 1, SEQ // 4, lengths)
    return lengths.astype(jnp.int32)


def level_of(rng, extent, pieces, smallest, high):
    def one(axis_at, shards_of):
        draws = jax.random.uniform(jax.random.fold_in(jax.random.fold_in(rng, 6), axis_at), (shards_of,), jnp.float32, smallest / len(pieces), high / len(pieces))
        return jnp.repeat(jnp.exp(draws), extent[axis_at] // shards_of).reshape((-1,) + (1,) * (len(extent) - axis_at - 1))

    loudness = one(*pieces[0])
    for cut in pieces[1:]:
        loudness = loudness * one(*cut)
    return loudness


def noise(rng, shape, deviation, most, shards=(), kind=jnp.bfloat16):
    drawn = deviation * jax.random.normal(rng, shape, jnp.float32)
    if shards:
        drawn = drawn * level_of(rng, shape, shards, -0.22, 0.18)
    return jnp.clip(drawn, -most, most).astype(kind)


def setup_inputs(seed: int = 0) -> dict:
    seeds = jax.random.split(jax.random.key(seed), 10)
    return {
        "cotangent": noise(seeds[0], (LAYERS, TOKENS, D), 1.0, 6.0, ((1, 128),)),
        "down_weight": noise(seeds[1], (LAYERS, FFW, D), D ** -0.5, 0.0625, ((0, 4), (1, 8), (2, 4))),
        "gate_act": jnp.clip(-0.25 + 2.75 * jax.random.uniform(seeds[2], (LAYERS, TOKENS, FFW), jnp.float32) ** level_of(seeds[2], (LAYERS, TOKENS, FFW), ((0, 4), (2, 8)), -0.2, 0.2), -0.25, 2.5).astype(jnp.bfloat16),
        "layer_input": noise(seeds[3], (LAYERS, TOKENS, D), 1.0, 6.0, ((0, 4), (1, 32))),
        "proj_out": noise(seeds[4], (LAYERS, KO, FFW), FFW ** -0.5, 0.046875, ((0, 4), (2, 8))),
        "proj_in": noise(seeds[5], (LAYERS, KI, D), D ** -0.5, 0.0625, ((0, 4),)),
        "queries": noise(seeds[6], (LAYERS, NQ, KP), KP ** -0.5, 0.09375, ((0, 4), (1, 32))),
        "hessian_prior": noise(seeds[7], (LAYERS, KP, KP), 0.5, 4.0, ((0, 4), (1, 32)), jnp.float32),
        "doc_lengths": draw_doc_lengths(jax.random.fold_in(seeds[9], 71), 0),
    }


def reference(cotangent, down_weight, gate_act, layer_input, proj_out, proj_in, queries, hessian_prior, doc_lengths):
    doc_scale = 1.0 / (SEQ ** 0.5)
    positions = jnp.arange(SEQ).astype(jnp.int32)
    valid_mask = (positions[None, :] < doc_lengths[:, None]).astype(jnp.float32)
    hessian_list = []
    score_total = jnp.zeros((NQ, DOCS), jnp.float32)
    for layer_index in range(LAYERS):
        hidden_grad = lax.dot_general(cotangent[layer_index], down_weight[layer_index], (((1,), (1,)), ((), ())), preferred_element_type=jnp.float32)
        up_grad = hidden_grad * gate_act[layer_index].astype(jnp.float32)
        out_rows = lax.dot_general(up_grad, proj_out[layer_index].astype(jnp.float32), (((1,), (1,)), ((), ())), precision=lax.Precision.HIGHEST)
        in_rows = lax.dot_general(layer_input[layer_index], proj_in[layer_index], (((1,), (1,)), ((), ())), preferred_element_type=jnp.float32)
        out_docs = out_rows.reshape(DOCS, SEQ, KO) * valid_mask[:, :, None]
        in_docs = in_rows.reshape(DOCS, SEQ, KI)
        projected = jnp.einsum("nta,ntb->nab", out_docs, in_docs, precision=lax.Precision.HIGHEST).reshape(DOCS, KO * KI) * doc_scale
        gram = lax.dot_general(projected, projected, (((0,), (0,)), ((), ())), precision=lax.Precision.HIGHEST)
        hessian_list.append(hessian_prior[layer_index] + gram / DOCS)
        score_total = score_total + lax.dot_general(queries[layer_index].astype(jnp.float32), projected, (((1,), (1,)), ((), ())), precision=lax.Precision.HIGHEST)
    return jnp.stack(hessian_list), score_total
```

```python
import jax
import jax.numpy as jnp
from jax import lax
from jax.sharding import PartitionSpec as P


def per_device(
    cotangent,
    down_weight,
    gate_act,
    layer_input,
    proj_out,
    proj_in,
    queries,
    hessian_prior,
    doc_lengths,
):
    layer_count, local_rows, model_width = cotangent.shape
    groups = lax.axis_size("example")
    shares = lax.axis_size("mp")
    col_width = model_width // groups
    pieces = cotangent.reshape(layer_count, local_rows, groups, col_width)
    pieces = jnp.transpose(pieces, (0, 2, 1, 3))
    pieces = jnp.broadcast_to(pieces[None], (shares,) + pieces.shape).reshape(
        shares * layer_count * groups, local_rows, col_width
    )
    routed = lax.all_to_all(
        pieces, ("mp", "layer", "example"), split_axis=0, concat_axis=1, tiled=True
    )
    token_cols = routed.reshape(-1, col_width)
    weight = down_weight[0]
    gate_rows = gate_act[0]
    out_project = proj_out[0].astype(jnp.float32)
    out_width = out_project.shape[0]
    own_rows = layer_input.shape[1]
    hidden_part = lax.dot_general(
        token_cols, weight, (((1,), (1,)), ((), ())), preferred_element_type=jnp.float32
    )
    scaled = hidden_part * gate_rows.astype(jnp.float32)
    out_part = lax.dot_general(
        scaled, out_project, (((1,), (1,)), ((), ())), precision=lax.Precision.HIGHEST
    )
    doc_devices = lax.axis_size(("mp", "example"))
    gathered = lax.all_to_all(
        out_part.reshape(doc_devices, own_rows, out_width),
        ("mp", "example"),
        split_axis=0,
        concat_axis=0,
        tiled=True,
    )
    out_rows = jnp.sum(gathered, axis=0)
    in_rows = lax.dot_general(
        layer_input[0], proj_in[0], (((1,), (1,)), ((), ())), preferred_element_type=jnp.float32
    )
    in_width = in_rows.shape[1]
    docs_here = doc_lengths.shape[0]
    seq_len = own_rows // docs_here
    doc_scale = 1.0 / seq_len**0.5
    positions = jnp.arange(seq_len)
    valid_mask = (positions[None, :] < doc_lengths[:, None]).astype(jnp.float32)
    out_docs = out_rows.reshape(docs_here, seq_len, out_width) * valid_mask[:, :, None]
    in_docs = in_rows.reshape(docs_here, seq_len, in_width)
    projected = (
        jnp.einsum("nta,ntb->nab", out_docs, in_docs, precision=lax.Precision.HIGHEST).reshape(
            docs_here, out_width * in_width
        )
        * doc_scale
    )
    all_docs = lax.all_gather(projected, ("mp", "example"), axis=0, tiled=True)
    doc_total = all_docs.shape[0]
    block_rows = hessian_prior.shape[1]
    first_col = lax.axis_index(("mp", "example")) * block_rows
    col_block = lax.dynamic_slice_in_dim(all_docs, first_col, block_rows, 1)
    gram_rows = lax.dot_general(
        col_block, all_docs, (((0,), (0,)), ((), ())), precision=lax.Precision.HIGHEST
    )
    hessian = hessian_prior[0] + gram_rows / doc_total
    score_part = lax.dot_general(
        queries[0].astype(jnp.float32),
        all_docs,
        (((1,), (1,)), ((), ())),
        precision=lax.Precision.HIGHEST,
    )
    scores = jnp.sum(lax.all_gather(score_part, "layer", axis=0), axis=0)
    return (hessian[None], scores)


def solution(mesh):
    in_specs = (
        P(None, ("mp", "layer", "example"), None),
        P("layer", "mp", "example"),
        P("layer", None, "mp"),
        P("layer", ("mp", "example"), None),
        P("layer", None, "mp"),
        P("layer", None, None),
        P("layer", ("mp", "example"), None),
        P("layer", ("mp", "example"), None),
        P(("mp", "example")),
    )
    out_specs = (P("layer", ("mp", "example"), None), P(("mp", "example"), None))
    return jax.shard_map(
        per_device, mesh=mesh, in_specs=in_specs, out_specs=out_specs, check_vma=False
    )
```

```python
import jax
import jax.numpy as jnp
from jax import lax
from jax.sharding import PartitionSpec as P
from jax.experimental import pallas as pl
from jax.experimental.pallas import tpu as pltpu


def _up_kernel(cot_ref, w_ref, gate_ref, proj_ref, out_ref):
    hidden = lax.dot_general(
        cot_ref[...], w_ref[...], (((1,), (1,)), ((), ())), preferred_element_type=jnp.float32
    )
    scaled = hidden * gate_ref[...].astype(jnp.float32)
    high = scaled.astype(jnp.bfloat16)
    low = (scaled - high.astype(jnp.float32)).astype(jnp.bfloat16)
    proj = proj_ref[...]
    dims = (((1,), (1,)), ((), ()))
    out_ref[...] = lax.dot_general(
        high, proj, dims, preferred_element_type=jnp.float32
    ) + lax.dot_general(low, proj, dims, preferred_element_type=jnp.float32)


def _up_project(token_cols, weight, gate_rows, proj):
    tokens, feats = token_cols.shape
    hidden = weight.shape[0]
    width = proj.shape[0]
    tile = 256
    return pl.pallas_call(
        _up_kernel,
        grid=(tokens // tile,),
        in_specs=[
            pl.BlockSpec((tile, feats), lambda i: (i, 0)),
            pl.BlockSpec((hidden, feats), lambda i: (0, 0)),
            pl.BlockSpec((tile, hidden), lambda i: (i, 0)),
            pl.BlockSpec((width, hidden), lambda i: (0, 0)),
        ],
        out_specs=pl.BlockSpec((tile, width), lambda i: (i, 0)),
        out_shape=jax.ShapeDtypeStruct((tokens, width), jnp.float32),
        compiler_params=pltpu.CompilerParams(vmem_limit_bytes=48 * 1024 * 1024),
    )(token_cols, weight, gate_rows, proj)


def per_device(
    cotangent,
    down_weight,
    gate_act,
    layer_input,
    proj_out,
    proj_in,
    queries,
    hessian_prior,
    doc_lengths,
):
    layer_count, local_rows, model_width = cotangent.shape
    groups = lax.axis_size("example")
    shares = lax.axis_size("mp")
    col_width = model_width // groups
    pieces = cotangent.reshape(layer_count, local_rows, groups, col_width)
    pieces = jnp.transpose(pieces, (0, 2, 1, 3))
    pieces = jnp.broadcast_to(pieces[None], (shares,) + pieces.shape).reshape(
        shares * layer_count * groups, local_rows, col_width
    )
    routed = lax.all_to_all(
        pieces, ("mp", "layer", "example"), split_axis=0, concat_axis=1, tiled=True
    )
    token_cols = routed.reshape(-1, col_width)
    out_width = proj_out.shape[1]
    own_rows = layer_input.shape[1]
    out_part = _up_project(token_cols, down_weight[0], gate_act[0], proj_out[0])
    doc_devices = lax.axis_size(("mp", "example"))
    gathered = lax.all_to_all(
        out_part.reshape(doc_devices, own_rows, out_width),
        ("mp", "example"),
        split_axis=0,
        concat_axis=0,
        tiled=True,
    )
    out_rows = jnp.sum(gathered, axis=0)
    in_rows = lax.dot_general(
        layer_input[0], proj_in[0], (((1,), (1,)), ((), ())), preferred_element_type=jnp.float32
    )
    in_width = in_rows.shape[1]
    docs_here = doc_lengths.shape[0]
    seq_len = own_rows // docs_here
    doc_scale = 1.0 / seq_len**0.5
    positions = jnp.arange(seq_len)
    valid_mask = (positions[None, :] < doc_lengths[:, None]).astype(jnp.float32)
    out_docs = out_rows.reshape(docs_here, seq_len, out_width) * valid_mask[:, :, None]
    in_docs = in_rows.reshape(docs_here, seq_len, in_width)
    projected = (
        jnp.einsum("nta,ntb->nab", out_docs, in_docs, precision=lax.Precision.HIGHEST).reshape(
            docs_here, out_width * in_width
        )
        * doc_scale
    )
    all_docs = lax.all_to_all(
        jnp.broadcast_to(projected, (doc_devices, projected.shape[1])),
        ("mp", "example"),
        split_axis=0,
        concat_axis=0,
        tiled=True,
    )
    doc_total = all_docs.shape[0]
    block_rows = hessian_prior.shape[1]
    first_col = lax.axis_index(("mp", "example")) * block_rows
    col_block = lax.dynamic_slice_in_dim(all_docs, first_col, block_rows, 1)
    gram_rows = lax.dot_general(
        col_block, all_docs, (((0,), (0,)), ((), ())), precision=lax.Precision.HIGHEST
    )
    hessian = hessian_prior[0] + gram_rows / doc_total
    score_part = lax.dot_general(
        queries[0].astype(jnp.float32),
        all_docs,
        (((1,), (1,)), ((), ())),
        precision=lax.Precision.HIGHEST,
    )
    layers = lax.axis_size("layer")
    scores = jnp.sum(
        lax.all_to_all(
            jnp.broadcast_to(score_part[None], (layers,) + score_part.shape),
            "layer",
            split_axis=0,
            concat_axis=0,
            tiled=True,
        ),
        axis=0,
    )
    return (hessian[None], scores)


def solution(mesh):
    in_specs = (
        P(None, ("mp", "layer", "example"), None),
        P("layer", "mp", "example"),
        P("layer", None, "mp"),
        P("layer", ("mp", "example"), None),
        P("layer", None, "mp"),
        P("layer", None, None),
        P("layer", ("mp", "example"), None),
        P("layer", ("mp", "example"), None),
        P(("mp", "example")),
    )
    out_specs = (P("layer", ("mp", "example"), None), P(("mp", "example"), None))
    return jax.shard_map(
        per_device, mesh=mesh, in_specs=in_specs, out_specs=out_specs, check_vma=False
    )
```

```python
import jax
import jax.numpy as jnp
from jax import lax
from jax.sharding import PartitionSpec as P
from jax.experimental import pallas as pl
from jax.experimental.pallas import tpu as pltpu


def _up_kernel(cot_ref, w_ref, gate_ref, proj_ref, out_ref):
    hidden = lax.dot_general(
        cot_ref[...], w_ref[...], (((1,), (1,)), ((), ())), preferred_element_type=jnp.float32
    )
    gate = gate_ref[...].astype(jnp.float32).reshape(hidden.shape)
    scaled = hidden * gate
    high = scaled.astype(jnp.bfloat16)
    low = (scaled - high.astype(jnp.float32)).astype(jnp.bfloat16)
    proj = proj_ref[...]
    dims = (((1,), (1,)), ((), ()))
    out_ref[...] = lax.dot_general(
        high, proj, dims, preferred_element_type=jnp.float32
    ) + lax.dot_general(low, proj, dims, preferred_element_type=jnp.float32)


def _up_project(token_cols, weight, gate4, chunk, proj):
    tokens, feats = token_cols.shape
    hidden = weight.shape[0]
    width = proj.shape[0]
    chunk_rows = gate4.shape[2]
    tile = 256
    per_tile = tile // chunk_rows
    return pl.pallas_call(
        _up_kernel,
        grid=(tokens // tile,),
        in_specs=[
            pl.BlockSpec((tile, feats), lambda i: (i, 0)),
            pl.BlockSpec((hidden, feats), lambda i: (0, 0)),
            pl.BlockSpec((per_tile, None, chunk_rows, hidden), lambda i: (i, chunk, 0, 0)),
            pl.BlockSpec((width, hidden), lambda i: (0, 0)),
        ],
        out_specs=pl.BlockSpec((tile, width), lambda i: (i, 0)),
        out_shape=jax.ShapeDtypeStruct((tokens, width), jnp.float32),
        compiler_params=pltpu.CompilerParams(vmem_limit_bytes=48 * 1024 * 1024),
    )(token_cols, weight, gate4, proj)


def per_device(
    cotangent,
    down_weight,
    gate_act,
    layer_input,
    proj_out,
    proj_in,
    queries,
    hessian_prior,
    doc_lengths,
):
    layer_count, local_rows, model_width = cotangent.shape
    groups = lax.axis_size("example")
    shares = lax.axis_size("mp")
    col_width = model_width // groups
    chunks = 2
    chunk_rows = local_rows // chunks
    pieces = cotangent.reshape(layer_count, chunks, chunk_rows, groups, col_width)
    pieces = jnp.transpose(pieces, (1, 0, 3, 2, 4))
    sources = shares * layer_count * groups
    out_width = proj_out.shape[1]
    own_rows = layer_input.shape[1]
    gate4 = gate_act[0].reshape(sources, chunks, chunk_rows, gate_act.shape[2])
    outs = []
    for c in range(chunks):
        piece = jnp.broadcast_to(pieces[c][None], (shares,) + pieces.shape[1:]).reshape(
            sources, chunk_rows, col_width
        )
        routed = lax.all_to_all(
            piece, ("mp", "layer", "example"), split_axis=0, concat_axis=0, tiled=True
        )
        outs.append(
            _up_project(routed.reshape(-1, col_width), down_weight[0], gate4, c, proj_out[0])
        )
    out_part = jnp.stack(outs).reshape(chunks, sources, chunk_rows, out_width)
    out_part = jnp.transpose(out_part, (1, 0, 2, 3)).reshape(-1, out_width)
    doc_devices = lax.axis_size(("mp", "example"))
    gathered = lax.all_to_all(
        out_part.reshape(doc_devices, own_rows, out_width),
        ("mp", "example"),
        split_axis=0,
        concat_axis=0,
        tiled=True,
    )
    out_rows = jnp.sum(gathered, axis=0)
    in_rows = lax.dot_general(
        layer_input[0], proj_in[0], (((1,), (1,)), ((), ())), preferred_element_type=jnp.float32
    )
    in_width = in_rows.shape[1]
    docs_here = doc_lengths.shape[0]
    seq_len = own_rows // docs_here
    doc_scale = 1.0 / seq_len**0.5
    positions = jnp.arange(seq_len)
    valid_mask = (positions[None, :] < doc_lengths[:, None]).astype(jnp.float32)
    out_docs = out_rows.reshape(docs_here, seq_len, out_width) * valid_mask[:, :, None]
    in_docs = in_rows.reshape(docs_here, seq_len, in_width)
    projected = (
        jnp.einsum("nta,ntb->nab", out_docs, in_docs, precision=lax.Precision.HIGHEST).reshape(
            docs_here, out_width * in_width
        )
        * doc_scale
    )
    all_docs = lax.all_to_all(
        jnp.broadcast_to(projected, (doc_devices, projected.shape[1])),
        ("mp", "example"),
        split_axis=0,
        concat_axis=0,
        tiled=True,
    )
    doc_total = all_docs.shape[0]
    block_rows = hessian_prior.shape[1]
    first_col = lax.axis_index(("mp", "example")) * block_rows
    col_block = lax.dynamic_slice_in_dim(all_docs, first_col, block_rows, 1)
    gram_rows = lax.dot_general(
        col_block, all_docs, (((0,), (0,)), ((), ())), precision=lax.Precision.HIGHEST
    )
    hessian = hessian_prior[0] + gram_rows / doc_total
    score_part = lax.dot_general(
        queries[0].astype(jnp.float32),
        all_docs,
        (((1,), (1,)), ((), ())),
        precision=lax.Precision.HIGHEST,
    )
    layers = lax.axis_size("layer")
    scores = jnp.sum(
        lax.all_to_all(
            jnp.broadcast_to(score_part[None], (layers,) + score_part.shape),
            "layer",
            split_axis=0,
            concat_axis=0,
            tiled=True,
        ),
        axis=0,
    )
    return (hessian[None], scores)


def solution(mesh):
    in_specs = (
        P(None, ("mp", "layer", "example"), None),
        P("layer", "mp", "example"),
        P("layer", None, "mp"),
        P("layer", ("mp", "example"), None),
        P("layer", None, "mp"),
        P("layer", None, None),
        P("layer", ("mp", "example"), None),
        P("layer", ("mp", "example"), None),
        P(("mp", "example")),
    )
    out_specs = (P("layer", ("mp", "example"), None), P(("mp", "example"), None))
    return jax.shard_map(
        per_device, mesh=mesh, in_specs=in_specs, out_specs=out_specs, check_vma=False
    )
```

```python
import jax
import jax.numpy as jnp
from jax import lax
from jax.sharding import PartitionSpec as P
from jax.experimental import pallas as pl
from jax.experimental.pallas import tpu as pltpu


def _up_kernel(cot_ref, w_ref, gate_ref, proj_ref, out_ref):
    hidden = lax.dot_general(
        cot_ref[...], w_ref[...], (((1,), (1,)), ((), ())), preferred_element_type=jnp.float32
    )
    layers, groups = gate_ref.shape[1], gate_ref.shape[2]
    gate = jnp.concatenate(
        [gate_ref[0, l, e] for e in range(groups) for l in range(layers)], axis=0
    ).astype(jnp.float32)
    scaled = hidden * gate
    high = scaled.astype(jnp.bfloat16)
    low = (scaled - high.astype(jnp.float32)).astype(jnp.bfloat16)
    proj = proj_ref[...]
    dims = (((1,), (1,)), ((), ()))
    out_ref[...] = lax.dot_general(
        high, proj, dims, preferred_element_type=jnp.float32
    ) + lax.dot_general(low, proj, dims, preferred_element_type=jnp.float32)


def _up_project(token_cols, weight, gate5, proj):
    tokens, feats = token_cols.shape
    hidden = weight.shape[0]
    width = proj.shape[0]
    blocks, layers, groups, rows = gate5.shape[:4]
    tile = tokens // blocks
    return pl.pallas_call(
        _up_kernel,
        grid=(blocks,),
        in_specs=[
            pl.BlockSpec((tile, feats), lambda i: (i, 0)),
            pl.BlockSpec((hidden, feats), lambda i: (0, 0)),
            pl.BlockSpec((1, layers, groups, rows, hidden), lambda i: (i, 0, 0, 0, 0)),
            pl.BlockSpec((width, hidden), lambda i: (0, 0)),
        ],
        out_specs=pl.BlockSpec((tile, width), lambda i: (i, 0)),
        out_shape=jax.ShapeDtypeStruct((tokens, width), jnp.float32),
        compiler_params=pltpu.CompilerParams(vmem_limit_bytes=48 * 1024 * 1024),
    )(token_cols, weight, gate5, proj)


def per_device(
    cotangent,
    down_weight,
    gate_act,
    layer_input,
    proj_out,
    proj_in,
    queries,
    hessian_prior,
    doc_lengths,
):
    layer_count, local_rows, model_width = cotangent.shape
    groups = lax.axis_size("example")
    shares = lax.axis_size("mp")
    col_width = model_width // groups
    pieces = cotangent.reshape(layer_count, local_rows, groups, col_width)
    pieces = jnp.transpose(pieces, (2, 0, 1, 3))
    pieces = jnp.broadcast_to(pieces[None], (shares,) + pieces.shape).reshape(
        shares * groups * layer_count, local_rows, col_width
    )
    routed = lax.all_to_all(
        pieces, ("mp", "example", "layer"), split_axis=0, concat_axis=0, tiled=True
    )
    token_cols = routed.reshape(-1, col_width)
    out_width = proj_out.shape[1]
    own_rows = layer_input.shape[1]
    gate5 = gate_act[0].reshape(shares, layer_count, groups, local_rows, gate_act.shape[2])
    out_part = _up_project(token_cols, down_weight[0], gate5, proj_out[0])
    out_part = jnp.transpose(
        out_part.reshape(shares, groups, layer_count, local_rows, out_width), (0, 2, 1, 3, 4)
    ).reshape(-1, out_width)
    doc_devices = lax.axis_size(("mp", "example"))
    gathered = lax.all_to_all(
        out_part.reshape(doc_devices, own_rows, out_width),
        ("mp", "example"),
        split_axis=0,
        concat_axis=0,
        tiled=True,
    )
    out_rows = jnp.sum(gathered, axis=0)
    in_rows = lax.dot_general(
        layer_input[0], proj_in[0], (((1,), (1,)), ((), ())), preferred_element_type=jnp.float32
    )
    in_width = in_rows.shape[1]
    docs_here = doc_lengths.shape[0]
    seq_len = own_rows // docs_here
    doc_scale = 1.0 / seq_len**0.5
    positions = jnp.arange(seq_len)
    valid_mask = (positions[None, :] < doc_lengths[:, None]).astype(jnp.float32)
    out_docs = out_rows.reshape(docs_here, seq_len, out_width) * valid_mask[:, :, None]
    in_docs = in_rows.reshape(docs_here, seq_len, in_width)
    projected = (
        jnp.einsum("nta,ntb->nab", out_docs, in_docs, precision=lax.Precision.HIGHEST).reshape(
            docs_here, out_width * in_width
        )
        * doc_scale
    )
    all_docs = lax.all_to_all(
        jnp.broadcast_to(projected, (doc_devices, projected.shape[1])),
        ("mp", "example"),
        split_axis=0,
        concat_axis=0,
        tiled=True,
    )
    doc_total = all_docs.shape[0]
    block_rows = hessian_prior.shape[1]
    first_col = lax.axis_index(("mp", "example")) * block_rows
    col_block = lax.dynamic_slice_in_dim(all_docs, first_col, block_rows, 1)
    gram_rows = lax.dot_general(
        col_block, all_docs, (((0,), (0,)), ((), ())), precision=lax.Precision.HIGHEST
    )
    hessian = hessian_prior[0] + gram_rows / doc_total
    score_part = lax.dot_general(
        queries[0].astype(jnp.float32),
        all_docs,
        (((1,), (1,)), ((), ())),
        precision=lax.Precision.HIGHEST,
    )
    layers = lax.axis_size("layer")
    scores = jnp.sum(
        lax.all_to_all(
            jnp.broadcast_to(score_part[None], (layers,) + score_part.shape),
            "layer",
            split_axis=0,
            concat_axis=0,
            tiled=True,
        ),
        axis=0,
    )
    return (hessian[None], scores)


def solution(mesh):
    in_specs = (
        P(None, ("mp", "layer", "example"), None),
        P("layer", "mp", "example"),
        P("layer", None, "mp"),
        P("layer", ("mp", "example"), None),
        P("layer", None, "mp"),
        P("layer", None, None),
        P("layer", ("mp", "example"), None),
        P("layer", ("mp", "example"), None),
        P(("mp", "example")),
    )
    out_specs = (P("layer", ("mp", "example"), None), P(("mp", "example"), None))
    return jax.shard_map(
        per_device, mesh=mesh, in_specs=in_specs, out_specs=out_specs, check_vma=False
    )
```

```python
import functools

import jax
import jax.numpy as jnp
from jax import lax
from jax.sharding import PartitionSpec as P
from jax.experimental import pallas as pl
from jax.experimental.pallas import tpu as pltpu


def _up_kernel(cot_ref, w_ref, gate_ref, proj_ref, out_ref, *, layer_major, lo, hi):
    hidden = lax.dot_general(
        cot_ref[...], w_ref[...], (((1,), (1,)), ((), ())), preferred_element_type=jnp.float32
    )
    blocks, layers, groups = gate_ref.shape[:3]
    if layer_major:
        order = [(b, l, e) for b in range(blocks) for l in range(layers) for e in range(groups)]
    else:
        order = [(b, l, e) for b in range(blocks) for e in range(groups) for l in range(layers)]
    gate = jnp.concatenate(
        [gate_ref[b, l, e].astype(jnp.float32)[lo:hi] for b, l, e in order], axis=0
    )
    scaled = hidden * gate
    high = scaled.astype(jnp.bfloat16)
    low = (scaled - high.astype(jnp.float32)).astype(jnp.bfloat16)
    proj = proj_ref[...]
    dims = (((1,), (1,)), ((), ()))
    out_ref[...] = lax.dot_general(
        high, proj, dims, preferred_element_type=jnp.float32
    ) + lax.dot_general(low, proj, dims, preferred_element_type=jnp.float32)


def _up_project(token_cols, weight, gate5, proj, layer_major, lo, hi):
    tokens, feats = token_cols.shape
    hidden = weight.shape[0]
    width = proj.shape[0]
    shares, layers, groups, rows = gate5.shape[:4]
    per_tile = 2
    tile = tokens // shares * per_tile
    kernel = functools.partial(_up_kernel, layer_major=layer_major, lo=lo, hi=hi)
    return pl.pallas_call(
        kernel,
        grid=(shares // per_tile,),
        in_specs=[
            pl.BlockSpec((tile, feats), lambda i: (i, 0)),
            pl.BlockSpec((hidden, feats), lambda i: (0, 0)),
            pl.BlockSpec((per_tile, layers, groups, rows, hidden), lambda i: (i, 0, 0, 0, 0)),
            pl.BlockSpec((width, hidden), lambda i: (0, 0)),
        ],
        out_specs=pl.BlockSpec((tile, width), lambda i: (i, 0)),
        out_shape=jax.ShapeDtypeStruct((tokens, width), jnp.float32),
        compiler_params=pltpu.CompilerParams(vmem_limit_bytes=48 * 1024 * 1024),
    )(token_cols, weight, gate5, proj)


def per_device(
    cotangent,
    down_weight,
    gate_act,
    layer_input,
    proj_out,
    proj_in,
    queries,
    hessian_prior,
    doc_lengths,
):
    layer_count, local_rows, model_width = cotangent.shape
    groups = lax.axis_size("example")
    shares = lax.axis_size("mp")
    col_width = model_width // groups
    split = local_rows // 2
    out_width = proj_out.shape[1]
    own_rows = layer_input.shape[1]
    gate5 = gate_act[0].reshape(shares, layer_count, groups, local_rows, gate_act.shape[2])
    near = cotangent[:, :split].reshape(layer_count, split, groups, col_width)
    near = jnp.transpose(near, (0, 2, 1, 3)).reshape(layer_count * groups, split, col_width)
    near = lax.all_to_all(near, ("layer", "example"), split_axis=0, concat_axis=0, tiled=True)
    near = lax.all_gather(near, "mp", axis=0, tiled=True)
    rest = local_rows - split
    far = cotangent[:, split:].reshape(layer_count, rest, groups, col_width)
    far = jnp.transpose(far, (2, 0, 1, 3))
    far = jnp.broadcast_to(far[None], (shares,) + far.shape).reshape(
        shares * groups * layer_count, rest, col_width
    )
    far = lax.all_to_all(far, ("mp", "example", "layer"), split_axis=0, concat_axis=0, tiled=True)
    far_out = _up_project(
        far.reshape(-1, col_width), down_weight[0], gate5, proj_out[0], False, split, local_rows
    )
    near_out = _up_project(
        near.reshape(-1, col_width), down_weight[0], gate5, proj_out[0], True, 0, split
    )
    far_out = jnp.transpose(
        far_out.reshape(shares, groups, layer_count, rest, out_width), (0, 2, 1, 3, 4)
    )
    near_out = near_out.reshape(shares, layer_count, groups, split, out_width)
    out_part = jnp.concatenate([near_out, far_out], axis=3).reshape(-1, out_width)
    doc_devices = lax.axis_size(("mp", "example"))
    gathered = lax.all_to_all(
        out_part.reshape(doc_devices, own_rows, out_width),
        ("mp", "example"),
        split_axis=0,
        concat_axis=0,
        tiled=True,
    )
    out_rows = jnp.sum(gathered, axis=0)
    in_rows = lax.dot_general(
        layer_input[0], proj_in[0], (((1,), (1,)), ((), ())), preferred_element_type=jnp.float32
    )
    in_width = in_rows.shape[1]
    docs_here = doc_lengths.shape[0]
    seq_len = own_rows // docs_here
    doc_scale = 1.0 / seq_len**0.5
    positions = jnp.arange(seq_len)
    valid_mask = (positions[None, :] < doc_lengths[:, None]).astype(jnp.float32)
    out_docs = out_rows.reshape(docs_here, seq_len, out_width) * valid_mask[:, :, None]
    in_docs = in_rows.reshape(docs_here, seq_len, in_width)
    projected = (
        jnp.einsum("nta,ntb->nab", out_docs, in_docs, precision=lax.Precision.HIGHEST).reshape(
            docs_here, out_width * in_width
        )
        * doc_scale
    )
    all_docs = lax.all_to_all(
        jnp.broadcast_to(projected, (doc_devices, projected.shape[1])),
        ("mp", "example"),
        split_axis=0,
        concat_axis=0,
        tiled=True,
    )
    doc_total = all_docs.shape[0]
    block_rows = hessian_prior.shape[1]
    first_col = lax.axis_index(("mp", "example")) * block_rows
    col_block = lax.dynamic_slice_in_dim(all_docs, first_col, block_rows, 1)
    gram_rows = lax.dot_general(
        col_block, all_docs, (((0,), (0,)), ((), ())), precision=lax.Precision.HIGHEST
    )
    hessian = hessian_prior[0] + gram_rows / doc_total
    score_part = lax.dot_general(
        queries[0].astype(jnp.float32),
        all_docs,
        (((1,), (1,)), ((), ())),
        precision=lax.Precision.HIGHEST,
    )
    layers = lax.axis_size("layer")
    scores = jnp.sum(
        lax.all_to_all(
            jnp.broadcast_to(score_part[None], (layers,) + score_part.shape),
            "layer",
            split_axis=0,
            concat_axis=0,
            tiled=True,
        ),
        axis=0,
    )
    return (hessian[None], scores)


def solution(mesh):
    in_specs = (
        P(None, ("mp", "layer", "example"), None),
        P("layer", "mp", "example"),
        P("layer", None, "mp"),
        P("layer", ("mp", "example"), None),
        P("layer", None, "mp"),
        P("layer", None, None),
        P("layer", ("mp", "example"), None),
        P("layer", ("mp", "example"), None),
        P(("mp", "example")),
    )
    out_specs = (P("layer", ("mp", "example"), None), P(("mp", "example"), None))
    return jax.shard_map(
        per_device, mesh=mesh, in_specs=in_specs, out_specs=out_specs, check_vma=False
    )
```

```python
import jax
import jax.numpy as jnp
from jax import lax
from jax.sharding import PartitionSpec as P
from jax.experimental import pallas as pl
from jax.experimental.pallas import tpu as pltpu


def _up_kernel(cot_ref, w_ref, gate_ref, proj_ref, out_ref):
    hidden = lax.dot_general(
        cot_ref[...], w_ref[...], (((1,), (1,)), ((), ())), preferred_element_type=jnp.float32
    )
    layers, groups = gate_ref.shape[1], gate_ref.shape[2]
    gate = jnp.concatenate(
        [gate_ref[0, l, e] for e in range(groups) for l in range(layers)], axis=0
    ).astype(jnp.float32)
    scaled = hidden * gate
    high = scaled.astype(jnp.bfloat16)
    low = (scaled - high.astype(jnp.float32)).astype(jnp.bfloat16)
    proj = proj_ref[...]
    dims = (((1,), (1,)), ((), ()))
    result = lax.dot_general(
        high, proj, dims, preferred_element_type=jnp.float32
    ) + lax.dot_general(low, proj, dims, preferred_element_type=jnp.float32)
    rows = gate_ref.shape[3]
    out_ref[...] = jnp.concatenate(
        [
            result[(e * layers + l) * rows : (e * layers + l + 1) * rows]
            for l in range(layers)
            for e in range(groups)
        ],
        axis=0,
    )


def _up_project(token_cols, weight, gate5, proj):
    tokens, feats = token_cols.shape
    hidden = weight.shape[0]
    width = proj.shape[0]
    blocks, layers, groups, rows = gate5.shape[:4]
    tile = tokens // blocks
    return pl.pallas_call(
        _up_kernel,
        grid=(blocks,),
        in_specs=[
            pl.BlockSpec((tile, feats), lambda i: (i, 0)),
            pl.BlockSpec((hidden, feats), lambda i: (0, 0)),
            pl.BlockSpec((1, layers, groups, rows, hidden), lambda i: (i, 0, 0, 0, 0)),
            pl.BlockSpec((width, hidden), lambda i: (0, 0)),
        ],
        out_specs=pl.BlockSpec((tile, width), lambda i: (i, 0)),
        out_shape=jax.ShapeDtypeStruct((tokens, width), jnp.float32),
        compiler_params=pltpu.CompilerParams(vmem_limit_bytes=48 * 1024 * 1024),
    )(token_cols, weight, gate5, proj)


def per_device(
    cotangent,
    down_weight,
    gate_act,
    layer_input,
    proj_out,
    proj_in,
    queries,
    hessian_prior,
    doc_lengths,
):
    layer_count, local_rows, model_width = cotangent.shape
    groups = lax.axis_size("example")
    shares = lax.axis_size("mp")
    col_width = model_width // groups
    pieces = cotangent.reshape(layer_count, local_rows, groups, col_width)
    pieces = jnp.transpose(pieces, (2, 0, 1, 3))
    pieces = jnp.broadcast_to(pieces[None], (shares,) + pieces.shape).reshape(
        shares * groups * layer_count, local_rows, col_width
    )
    routed = lax.all_to_all(
        pieces, ("mp", "example", "layer"), split_axis=0, concat_axis=0, tiled=True
    )
    token_cols = routed.reshape(-1, col_width)
    out_width = proj_out.shape[1]
    own_rows = layer_input.shape[1]
    gate5 = gate_act[0].reshape(shares, layer_count, groups, local_rows, gate_act.shape[2])
    out_part = _up_project(token_cols, down_weight[0], gate5, proj_out[0])
    doc_devices = lax.axis_size(("mp", "example"))
    gathered = lax.all_to_all(
        out_part.reshape(doc_devices, own_rows, out_width),
        ("mp", "example"),
        split_axis=0,
        concat_axis=0,
        tiled=True,
    )
    out_rows = jnp.sum(gathered, axis=0)
    in_rows = lax.dot_general(
        layer_input[0], proj_in[0], (((1,), (1,)), ((), ())), preferred_element_type=jnp.float32
    )
    in_width = in_rows.shape[1]
    docs_here = doc_lengths.shape[0]
    seq_len = own_rows // docs_here
    doc_scale = 1.0 / seq_len**0.5
    positions = jnp.arange(seq_len)
    valid_mask = (positions[None, :] < doc_lengths[:, None]).astype(jnp.float32)
    out_docs = out_rows.reshape(docs_here, seq_len, out_width) * valid_mask[:, :, None]
    in_docs = in_rows.reshape(docs_here, seq_len, in_width)
    projected = (
        jnp.einsum("nta,ntb->nab", out_docs, in_docs, precision=lax.Precision.HIGHEST).reshape(
            docs_here, out_width * in_width
        )
        * doc_scale
    )
    all_docs = lax.all_to_all(
        jnp.broadcast_to(projected, (doc_devices, projected.shape[1])),
        ("mp", "example"),
        split_axis=0,
        concat_axis=0,
        tiled=True,
    )
    doc_total = all_docs.shape[0]
    block_rows = hessian_prior.shape[1]
    first_col = lax.axis_index(("mp", "example")) * block_rows
    col_block = lax.dynamic_slice_in_dim(all_docs, first_col, block_rows, 1)
    gram_rows = lax.dot_general(
        col_block, all_docs, (((0,), (0,)), ((), ())), precision=lax.Precision.HIGHEST
    )
    hessian = hessian_prior[0] + gram_rows / doc_total
    score_part = lax.dot_general(
        queries[0].astype(jnp.float32),
        all_docs,
        (((1,), (1,)), ((), ())),
        precision=lax.Precision.HIGHEST,
    )
    layers = lax.axis_size("layer")
    scores = jnp.sum(
        lax.all_to_all(
            jnp.broadcast_to(score_part[None], (layers,) + score_part.shape),
            "layer",
            split_axis=0,
            concat_axis=0,
            tiled=True,
        ),
        axis=0,
    )
    return (hessian[None], scores)


def solution(mesh):
    in_specs = (
        P(None, ("mp", "layer", "example"), None),
        P("layer", "mp", "example"),
        P("layer", None, "mp"),
        P("layer", ("mp", "example"), None),
        P("layer", None, "mp"),
        P("layer", None, None),
        P("layer", ("mp", "example"), None),
        P("layer", ("mp", "example"), None),
        P(("mp", "example")),
    )
    out_specs = (P("layer", ("mp", "example"), None), P(("mp", "example"), None))
    return jax.shard_map(
        per_device, mesh=mesh, in_specs=in_specs, out_specs=out_specs, check_vma=False
    )
```

```python
import jax
import jax.numpy as jnp
from jax import lax
from jax.sharding import PartitionSpec as P
from jax.experimental import pallas as pl
from jax.experimental.pallas import tpu as pltpu


def _up_kernel(cot_ref, w_ref, gate_ref, proj_ref, out_ref):
    hidden = lax.dot_general(
        cot_ref[...], w_ref[...], (((1,), (1,)), ((), ())), preferred_element_type=jnp.float32
    )
    blocks, layers, groups = gate_ref.shape[:3]
    gate = jnp.concatenate(
        [
            gate_ref[b, l, e]
            for b in range(blocks)
            for e in range(groups)
            for l in range(layers)
        ],
        axis=0,
    ).astype(jnp.float32)
    scaled = hidden * gate
    high = scaled.astype(jnp.bfloat16)
    low = (scaled - high.astype(jnp.float32)).astype(jnp.bfloat16)
    proj = proj_ref[...]
    dims = (((1,), (1,)), ((), ()))
    result = lax.dot_general(
        high, proj, dims, preferred_element_type=jnp.float32
    ) + lax.dot_general(low, proj, dims, preferred_element_type=jnp.float32)
    rows = gate_ref.shape[3]
    out_ref[...] = jnp.concatenate(
        [
            result[((b * groups + e) * layers + l) * rows :][:rows]
            for b in range(blocks)
            for l in range(layers)
            for e in range(groups)
        ],
        axis=0,
    )


def _up_project(token_cols, weight, gate5, proj):
    tokens, feats = token_cols.shape
    hidden = weight.shape[0]
    width = proj.shape[0]
    shares, layers, groups, rows = gate5.shape[:4]
    per_tile = 2
    blocks = shares // per_tile
    tile = tokens // blocks
    return pl.pallas_call(
        _up_kernel,
        grid=(blocks,),
        in_specs=[
            pl.BlockSpec((tile, feats), lambda i: (i, 0)),
            pl.BlockSpec((hidden, feats), lambda i: (0, 0)),
            pl.BlockSpec((per_tile, layers, groups, rows, hidden), lambda i: (i, 0, 0, 0, 0)),
            pl.BlockSpec((width, hidden), lambda i: (0, 0)),
        ],
        out_specs=pl.BlockSpec((tile, width), lambda i: (i, 0)),
        out_shape=jax.ShapeDtypeStruct((tokens, width), jnp.float32),
        compiler_params=pltpu.CompilerParams(vmem_limit_bytes=48 * 1024 * 1024),
    )(token_cols, weight, gate5, proj)


def per_device(
    cotangent,
    down_weight,
    gate_act,
    layer_input,
    proj_out,
    proj_in,
    queries,
    hessian_prior,
    doc_lengths,
):
    layer_count, local_rows, model_width = cotangent.shape
    groups = lax.axis_size("example")
    shares = lax.axis_size("mp")
    col_width = model_width // groups
    pieces = cotangent.reshape(layer_count, local_rows, groups, col_width)
    pieces = jnp.transpose(pieces, (2, 0, 1, 3))
    pieces = jnp.broadcast_to(pieces[None], (shares,) + pieces.shape).reshape(
        shares * groups * layer_count, local_rows, col_width
    )
    routed = lax.all_to_all(
        pieces, ("mp", "example", "layer"), split_axis=0, concat_axis=0, tiled=True
    )
    token_cols = routed.reshape(-1, col_width)
    out_width = proj_out.shape[1]
    own_rows = layer_input.shape[1]
    gate5 = gate_act[0].reshape(shares, layer_count, groups, local_rows, gate_act.shape[2])
    out_part = _up_project(token_cols, down_weight[0], gate5, proj_out[0])
    doc_devices = lax.axis_size(("mp", "example"))
    gathered = lax.all_to_all(
        out_part.reshape(doc_devices, own_rows, out_width),
        ("mp", "example"),
        split_axis=0,
        concat_axis=0,
        tiled=True,
    )
    out_rows = jnp.sum(gathered, axis=0)
    in_rows = lax.dot_general(
        layer_input[0], proj_in[0], (((1,), (1,)), ((), ())), preferred_element_type=jnp.float32
    )
    in_width = in_rows.shape[1]
    docs_here = doc_lengths.shape[0]
    seq_len = own_rows // docs_here
    doc_scale = 1.0 / seq_len**0.5
    positions = jnp.arange(seq_len)
    valid_mask = (positions[None, :] < doc_lengths[:, None]).astype(jnp.float32)
    out_docs = out_rows.reshape(docs_here, seq_len, out_width) * valid_mask[:, :, None]
    in_docs = in_rows.reshape(docs_here, seq_len, in_width)
    projected = (
        jnp.einsum("nta,ntb->nab", out_docs, in_docs, precision=lax.Precision.HIGHEST).reshape(
            docs_here, out_width * in_width
        )
        * doc_scale
    )
    all_docs = lax.all_to_all(
        jnp.broadcast_to(projected, (doc_devices, projected.shape[1])),
        ("mp", "example"),
        split_axis=0,
        concat_axis=0,
        tiled=True,
    )
    doc_total = all_docs.shape[0]
    block_rows = hessian_prior.shape[1]
    first_col = lax.axis_index(("mp", "example")) * block_rows
    col_block = lax.dynamic_slice_in_dim(all_docs, first_col, block_rows, 1)
    gram_rows = lax.dot_general(
        col_block, all_docs, (((0,), (0,)), ((), ())), precision=lax.Precision.HIGHEST
    )
    hessian = hessian_prior[0] + gram_rows / doc_total
    score_part = lax.dot_general(
        queries[0].astype(jnp.float32),
        all_docs,
        (((1,), (1,)), ((), ())),
        precision=lax.Precision.HIGHEST,
    )
    layers = lax.axis_size("layer")
    scores = jnp.sum(
        lax.all_to_all(
            jnp.broadcast_to(score_part[None], (layers,) + score_part.shape),
            "layer",
            split_axis=0,
            concat_axis=0,
            tiled=True,
        ),
        axis=0,
    )
    return (hessian[None], scores)


def solution(mesh):
    in_specs = (
        P(None, ("mp", "layer", "example"), None),
        P("layer", "mp", "example"),
        P("layer", None, "mp"),
        P("layer", ("mp", "example"), None),
        P("layer", None, "mp"),
        P("layer", None, None),
        P("layer", ("mp", "example"), None),
        P("layer", ("mp", "example"), None),
        P(("mp", "example")),
    )
    out_specs = (P("layer", ("mp", "example"), None), P(("mp", "example"), None))
    return jax.shard_map(
        per_device, mesh=mesh, in_specs=in_specs, out_specs=out_specs, check_vma=False
    )
```

```python
import jax
import jax.numpy as jnp
from jax import lax
from jax.sharding import PartitionSpec as P
from jax.experimental import pallas as pl
from jax.experimental.pallas import tpu as pltpu


def _up_kernel(cot_ref, w_ref, gate_ref, proj_ref, out_ref):
    hidden = lax.dot_general(
        cot_ref[...], w_ref[...], (((1,), (1,)), ((), ())), preferred_element_type=jnp.float32
    )
    blocks, layers, groups = gate_ref.shape[:3]
    gate = jnp.concatenate(
        [
            gate_ref[b, l, e]
            for b in range(blocks)
            for e in range(groups)
            for l in range(layers)
        ],
        axis=0,
    ).astype(jnp.float32)
    scaled = hidden * gate
    high = scaled.astype(jnp.bfloat16)
    low = (scaled - high.astype(jnp.float32)).astype(jnp.bfloat16)
    proj = proj_ref[...]
    dims = (((1,), (1,)), ((), ()))
    result = lax.dot_general(
        high, proj, dims, preferred_element_type=jnp.float32
    ) + lax.dot_general(low, proj, dims, preferred_element_type=jnp.float32)
    rows = gate_ref.shape[3]
    out_ref[...] = jnp.concatenate(
        [
            result[((b * groups + e) * layers + l) * rows :][:rows]
            for b in range(blocks)
            for l in range(layers)
            for e in range(groups)
        ],
        axis=0,
    )


def _up_project(token_cols, weight, gate5, proj):
    tokens, feats = token_cols.shape
    hidden = weight.shape[0]
    width = proj.shape[0]
    shares, layers, groups, rows = gate5.shape[:4]
    per_tile = 2
    blocks = shares // per_tile
    tile = tokens // blocks
    return pl.pallas_call(
        _up_kernel,
        grid=(blocks,),
        in_specs=[
            pl.BlockSpec((tile, feats), lambda i: (i, 0)),
            pl.BlockSpec((hidden, feats), lambda i: (0, 0)),
            pl.BlockSpec((per_tile, layers, groups, rows, hidden), lambda i: (i, 0, 0, 0, 0)),
            pl.BlockSpec((width, hidden), lambda i: (0, 0)),
        ],
        out_specs=pl.BlockSpec((tile, width), lambda i: (i, 0)),
        out_shape=jax.ShapeDtypeStruct((tokens, width), jnp.float32),
        compiler_params=pltpu.CompilerParams(vmem_limit_bytes=48 * 1024 * 1024),
    )(token_cols, weight, gate5, proj)


def per_device(
    cotangent,
    down_weight,
    gate_act,
    layer_input,
    proj_out,
    proj_in,
    queries,
    hessian_prior,
    doc_lengths,
):
    layer_count, local_rows, model_width = cotangent.shape
    groups = lax.axis_size("example")
    shares = lax.axis_size("mp")
    col_width = model_width // groups
    pieces = jnp.stack(
        [cotangent[:, :, e * col_width : (e + 1) * col_width] for e in range(groups)]
    )
    pieces = jnp.broadcast_to(pieces[None], (shares,) + pieces.shape).reshape(
        shares * groups * layer_count, local_rows, col_width
    )
    routed = lax.all_to_all(
        pieces, ("mp", "example", "layer"), split_axis=0, concat_axis=0, tiled=True
    )
    token_cols = routed.reshape(-1, col_width)
    out_width = proj_out.shape[1]
    own_rows = layer_input.shape[1]
    gate5 = gate_act[0].reshape(shares, layer_count, groups, local_rows, gate_act.shape[2])
    out_part = _up_project(token_cols, down_weight[0], gate5, proj_out[0])
    doc_devices = lax.axis_size(("mp", "example"))
    gathered = lax.all_to_all(
        out_part.reshape(doc_devices, own_rows, out_width),
        ("mp", "example"),
        split_axis=0,
        concat_axis=0,
        tiled=True,
    )
    out_rows = jnp.sum(gathered, axis=0)
    in_rows = lax.dot_general(
        layer_input[0], proj_in[0], (((1,), (1,)), ((), ())), preferred_element_type=jnp.float32
    )
    in_width = in_rows.shape[1]
    docs_here = doc_lengths.shape[0]
    seq_len = own_rows // docs_here
    doc_scale = 1.0 / seq_len**0.5
    positions = jnp.arange(seq_len)
    valid_mask = (positions[None, :] < doc_lengths[:, None]).astype(jnp.float32)
    out_docs = out_rows.reshape(docs_here, seq_len, out_width) * valid_mask[:, :, None]
    in_docs = in_rows.reshape(docs_here, seq_len, in_width)
    projected = (
        jnp.einsum("nta,ntb->nab", out_docs, in_docs, precision=lax.Precision.HIGHEST).reshape(
            docs_here, out_width * in_width
        )
        * doc_scale
    )
    all_docs = lax.all_to_all(
        jnp.broadcast_to(projected, (doc_devices, projected.shape[1])),
        ("mp", "example"),
        split_axis=0,
        concat_axis=0,
        tiled=True,
    )
    doc_total = all_docs.shape[0]
    block_rows = hessian_prior.shape[1]
    first_col = lax.axis_index(("mp", "example")) * block_rows
    col_block = lax.dynamic_slice_in_dim(all_docs, first_col, block_rows, 1)
    gram_rows = lax.dot_general(
        col_block, all_docs, (((0,), (0,)), ((), ())), precision=lax.Precision.HIGHEST
    )
    hessian = hessian_prior[0] + gram_rows / doc_total
    score_part = lax.dot_general(
        queries[0].astype(jnp.float32),
        all_docs,
        (((1,), (1,)), ((), ())),
        precision=lax.Precision.HIGHEST,
    )
    layers = lax.axis_size("layer")
    scores = jnp.sum(
        lax.all_to_all(
            jnp.broadcast_to(score_part[None], (layers,) + score_part.shape),
            "layer",
            split_axis=0,
            concat_axis=0,
            tiled=True,
        ),
        axis=0,
    )
    return (hessian[None], scores)


def solution(mesh):
    in_specs = (
        P(None, ("mp", "layer", "example"), None),
        P("layer", "mp", "example"),
        P("layer", None, "mp"),
        P("layer", ("mp", "example"), None),
        P("layer", None, "mp"),
        P("layer", None, None),
        P("layer", ("mp", "example"), None),
        P("layer", ("mp", "example"), None),
        P(("mp", "example")),
    )
    out_specs = (P("layer", ("mp", "example"), None), P(("mp", "example"), None))
    return jax.shard_map(
        per_device, mesh=mesh, in_specs=in_specs, out_specs=out_specs, check_vma=False
    )
```

```python
import jax
import jax.numpy as jnp
from jax import lax
from jax.sharding import PartitionSpec as P
from jax.experimental import pallas as pl
from jax.experimental.pallas import tpu as pltpu


def _up_kernel(cot_ref, w_ref, gate_ref, proj_ref, out_ref):
    hidden = lax.dot_general(
        cot_ref[...], w_ref[...], (((1,), (1,)), ((), ())), preferred_element_type=jnp.float32
    )
    blocks, layers, groups = gate_ref.shape[:3]
    gate = jnp.concatenate(
        [
            gate_ref[b, l, e]
            for b in range(blocks)
            for e in range(groups)
            for l in range(layers)
        ],
        axis=0,
    ).astype(jnp.float32)
    scaled = hidden * gate
    high = scaled.astype(jnp.bfloat16)
    low = (scaled - high.astype(jnp.float32)).astype(jnp.bfloat16)
    proj = proj_ref[...]
    dims = (((1,), (1,)), ((), ()))
    result = lax.dot_general(
        high, proj, dims, preferred_element_type=jnp.float32
    ) + lax.dot_general(low, proj, dims, preferred_element_type=jnp.float32)
    rows = gate_ref.shape[3]
    out_ref[...] = jnp.concatenate(
        [
            result[((b * groups + e) * layers + l) * rows :][:rows]
            for b in range(blocks)
            for l in range(layers)
            for e in range(groups)
        ],
        axis=0,
    )


def _up_project(token_cols, weight, gate5, proj):
    tokens, feats = token_cols.shape
    hidden = weight.shape[0]
    width = proj.shape[0]
    shares, layers, groups, rows = gate5.shape[:4]
    per_tile = 2
    blocks = shares // per_tile
    tile = tokens // blocks
    return pl.pallas_call(
        _up_kernel,
        grid=(blocks,),
        in_specs=[
            pl.BlockSpec((tile, feats), lambda i: (i, 0)),
            pl.BlockSpec((hidden, feats), lambda i: (0, 0)),
            pl.BlockSpec((per_tile, layers, groups, rows, hidden), lambda i: (i, 0, 0, 0, 0)),
            pl.BlockSpec((width, hidden), lambda i: (0, 0)),
        ],
        out_specs=pl.BlockSpec((tile, width), lambda i: (i, 0)),
        out_shape=jax.ShapeDtypeStruct((tokens, width), jnp.float32),
        compiler_params=pltpu.CompilerParams(vmem_limit_bytes=48 * 1024 * 1024),
    )(token_cols, weight, gate5, proj)


def per_device(
    cotangent,
    down_weight,
    gate_act,
    layer_input,
    proj_out,
    proj_in,
    queries,
    hessian_prior,
    doc_lengths,
):
    layer_count, local_rows, model_width = cotangent.shape
    groups = lax.axis_size("example")
    shares = lax.axis_size("mp")
    col_width = model_width // groups
    pieces = jnp.stack(
        [cotangent[:, :, e * col_width : (e + 1) * col_width] for e in range(groups)]
    )
    pieces = jnp.broadcast_to(pieces[None], (shares,) + pieces.shape).reshape(
        shares * groups * layer_count, local_rows, col_width
    )
    routed = lax.all_to_all(
        pieces, ("mp", "example", "layer"), split_axis=0, concat_axis=0, tiled=True
    )
    token_cols = routed.reshape(-1, col_width)
    out_width = proj_out.shape[1]
    own_rows = layer_input.shape[1]
    gate5 = gate_act[0].reshape(shares, layer_count, groups, local_rows, gate_act.shape[2])
    out_part = _up_project(token_cols, down_weight[0], gate5, proj_out[0])
    doc_devices = lax.axis_size(("mp", "example"))
    gathered = lax.all_to_all(
        out_part.reshape(doc_devices, 8, own_rows * out_width // 8),
        ("mp", "example"),
        split_axis=0,
        concat_axis=0,
        tiled=True,
    )
    out_rows = jnp.sum(gathered, axis=0).reshape(own_rows, out_width)
    in_rows = lax.dot_general(
        layer_input[0], proj_in[0], (((1,), (1,)), ((), ())), preferred_element_type=jnp.float32
    )
    in_width = in_rows.shape[1]
    docs_here = doc_lengths.shape[0]
    seq_len = own_rows // docs_here
    doc_scale = 1.0 / seq_len**0.5
    positions = jnp.arange(seq_len)
    valid_mask = (positions[None, :] < doc_lengths[:, None]).astype(jnp.float32)
    out_docs = out_rows.reshape(docs_here, seq_len, out_width) * valid_mask[:, :, None]
    in_docs = in_rows.reshape(docs_here, seq_len, in_width)
    projected = (
        jnp.einsum("nta,ntb->nab", out_docs, in_docs, precision=lax.Precision.HIGHEST).reshape(
            docs_here, out_width * in_width
        )
        * doc_scale
    )
    all_docs = lax.all_to_all(
        jnp.broadcast_to(projected, (doc_devices, projected.shape[1])),
        ("mp", "example"),
        split_axis=0,
        concat_axis=0,
        tiled=True,
    )
    doc_total = all_docs.shape[0]
    block_rows = hessian_prior.shape[1]
    first_col = lax.axis_index(("mp", "example")) * block_rows
    col_block = lax.dynamic_slice_in_dim(all_docs, first_col, block_rows, 1)
    gram_rows = lax.dot_general(
        col_block, all_docs, (((0,), (0,)), ((), ())), precision=lax.Precision.HIGHEST
    )
    hessian = hessian_prior[0] + gram_rows / doc_total
    score_part = lax.dot_general(
        queries[0].astype(jnp.float32),
        all_docs,
        (((1,), (1,)), ((), ())),
        precision=lax.Precision.HIGHEST,
    )
    layers = lax.axis_size("layer")
    scores = jnp.sum(
        lax.all_to_all(
            jnp.broadcast_to(score_part[None], (layers,) + score_part.shape),
            "layer",
            split_axis=0,
            concat_axis=0,
            tiled=True,
        ),
        axis=0,
    )
    return (hessian[None], scores)


def solution(mesh):
    in_specs = (
        P(None, ("mp", "layer", "example"), None),
        P("layer", "mp", "example"),
        P("layer", None, "mp"),
        P("layer", ("mp", "example"), None),
        P("layer", None, "mp"),
        P("layer", None, None),
        P("layer", ("mp", "example"), None),
        P("layer", ("mp", "example"), None),
        P(("mp", "example")),
    )
    out_specs = (P("layer", ("mp", "example"), None), P(("mp", "example"), None))
    return jax.shard_map(
        per_device, mesh=mesh, in_specs=in_specs, out_specs=out_specs, check_vma=False
    )
```

```python
import jax
import jax.numpy as jnp
from jax import lax
from jax.sharding import PartitionSpec as P
from jax.experimental import pallas as pl
from jax.experimental.pallas import tpu as pltpu


def _up_kernel(cot_ref, w_ref, gate_ref, proj_ref, out_ref):
    hidden = lax.dot_general(
        cot_ref[...], w_ref[...], (((1,), (1,)), ((), ())), preferred_element_type=jnp.float32
    )
    blocks, layers, groups = gate_ref.shape[:3]
    gate = jnp.concatenate(
        [
            gate_ref[b, l, e]
            for b in range(blocks)
            for e in range(groups)
            for l in range(layers)
        ],
        axis=0,
    ).astype(jnp.float32)
    scaled = hidden * gate
    high = scaled.astype(jnp.bfloat16)
    low = (scaled - high.astype(jnp.float32)).astype(jnp.bfloat16)
    proj = proj_ref[...]
    dims = (((1,), (1,)), ((), ()))
    result = lax.dot_general(
        high, proj, dims, preferred_element_type=jnp.float32
    ) + lax.dot_general(low, proj, dims, preferred_element_type=jnp.float32)
    rows = gate_ref.shape[3]
    out_ref[...] = jnp.concatenate(
        [
            result[((b * groups + e) * layers + l) * rows :][:rows]
            for b in range(blocks)
            for l in range(layers)
            for e in range(groups)
        ],
        axis=0,
    )


def _up_project(token_cols, weight, gate5, proj):
    tokens, feats = token_cols.shape
    hidden = weight.shape[0]
    width = proj.shape[0]
    shares, layers, groups, rows = gate5.shape[:4]
    per_tile = 2
    blocks = shares // per_tile
    tile = tokens // blocks
    return pl.pallas_call(
        _up_kernel,
        grid=(blocks,),
        in_specs=[
            pl.BlockSpec((tile, feats), lambda i: (i, 0)),
            pl.BlockSpec((hidden, feats), lambda i: (0, 0)),
            pl.BlockSpec((per_tile, layers, groups, rows, hidden), lambda i: (i, 0, 0, 0, 0)),
            pl.BlockSpec((width, hidden), lambda i: (0, 0)),
        ],
        out_specs=pl.BlockSpec((tile, width), lambda i: (i, 0)),
        out_shape=jax.ShapeDtypeStruct((tokens, width), jnp.float32),
        compiler_params=pltpu.CompilerParams(vmem_limit_bytes=48 * 1024 * 1024),
    )(token_cols, weight, gate5, proj)


def per_device(
    cotangent,
    down_weight,
    gate_act,
    layer_input,
    proj_out,
    proj_in,
    queries,
    hessian_prior,
    doc_lengths,
):
    layer_count, local_rows, model_width = cotangent.shape
    groups = lax.axis_size("example")
    shares = lax.axis_size("mp")
    col_width = model_width // groups
    pieces = jnp.stack(
        [cotangent[:, :, e * col_width : (e + 1) * col_width] for e in range(groups)]
    )
    pieces = jnp.broadcast_to(pieces[None], (shares,) + pieces.shape).reshape(
        shares * groups * layer_count, local_rows, col_width
    )
    routed = lax.all_to_all(
        pieces, ("mp", "example", "layer"), split_axis=0, concat_axis=0, tiled=True
    )
    token_cols = routed.reshape(-1, col_width)
    out_width = proj_out.shape[1]
    own_rows = layer_input.shape[1]
    gate5 = gate_act[0].reshape(shares, layer_count, groups, local_rows, gate_act.shape[2])
    out_part = _up_project(token_cols, down_weight[0], gate5, proj_out[0])
    doc_devices = lax.axis_size(("mp", "example"))
    gathered = lax.all_to_all(
        out_part.reshape(doc_devices, 8, own_rows * out_width // 8),
        ("mp", "example"),
        split_axis=0,
        concat_axis=0,
        tiled=True,
    )
    out_rows = jnp.sum(gathered, axis=0).reshape(own_rows, out_width)
    in_rows = lax.dot_general(
        layer_input[0], proj_in[0], (((1,), (1,)), ((), ())), preferred_element_type=jnp.float32
    )
    in_width = in_rows.shape[1]
    docs_here = doc_lengths.shape[0]
    seq_len = own_rows // docs_here
    doc_scale = 1.0 / seq_len**0.5
    positions = jnp.arange(seq_len)
    valid_mask = (positions[None, :] < doc_lengths[:, None]).astype(jnp.float32)
    out_docs = out_rows.reshape(docs_here, seq_len, out_width) * valid_mask[:, :, None]
    in_docs = in_rows.reshape(docs_here, seq_len, in_width)
    projected = (
        jnp.einsum("nta,ntb->nab", out_docs, in_docs, precision=lax.Precision.HIGHEST).reshape(
            docs_here, out_width * in_width
        )
        * doc_scale
    )
    doc_width = projected.shape[1]
    all_docs = lax.all_to_all(
        jnp.broadcast_to(projected.reshape(1, 8, doc_width // 8), (doc_devices, 8, doc_width // 8)),
        ("mp", "example"),
        split_axis=0,
        concat_axis=0,
        tiled=True,
    ).reshape(doc_devices, doc_width)
    doc_total = all_docs.shape[0]
    block_rows = hessian_prior.shape[1]
    first_col = lax.axis_index(("mp", "example")) * block_rows
    col_block = lax.dynamic_slice_in_dim(all_docs, first_col, block_rows, 1)
    gram_rows = lax.dot_general(
        col_block, all_docs, (((0,), (0,)), ((), ())), precision=lax.Precision.HIGHEST
    )
    hessian = hessian_prior[0] + gram_rows / doc_total
    score_part = lax.dot_general(
        queries[0].astype(jnp.float32),
        all_docs,
        (((1,), (1,)), ((), ())),
        precision=lax.Precision.HIGHEST,
    )
    layers = lax.axis_size("layer")
    score_size = score_part.size
    scores = jnp.sum(
        lax.all_to_all(
            jnp.broadcast_to(score_part.reshape(1, 8, score_size // 8), (layers, 8, score_size // 8)),
            "layer",
            split_axis=0,
            concat_axis=0,
            tiled=True,
        ),
        axis=0,
    ).reshape(score_part.shape)
    return (hessian[None], scores)


def solution(mesh):
    in_specs = (
        P(None, ("mp", "layer", "example"), None),
        P("layer", "mp", "example"),
        P("layer", None, "mp"),
        P("layer", ("mp", "example"), None),
        P("layer", None, "mp"),
        P("layer", None, None),
        P("layer", ("mp", "example"), None),
        P("layer", ("mp", "example"), None),
        P(("mp", "example")),
    )
    out_specs = (P("layer", ("mp", "example"), None), P(("mp", "example"), None))
    return jax.shard_map(
        per_device, mesh=mesh, in_specs=in_specs, out_specs=out_specs, check_vma=False
    )
```

```python
import jax
import jax.numpy as jnp
from jax import lax
from jax.sharding import PartitionSpec as P
from jax.experimental import pallas as pl
from jax.experimental.pallas import tpu as pltpu


def _up_kernel(cot_ref, w_ref, gate_ref, proj_ref, out_ref, order_ref):
    hidden = lax.dot_general(
        cot_ref[...], w_ref[...], (((1,), (1,)), ((), ())), preferred_element_type=jnp.float32
    )
    blocks, layers, groups = gate_ref.shape[:3]
    gate = jnp.concatenate(
        [
            gate_ref[b, l, e]
            for b in range(blocks)
            for e in range(groups)
            for l in range(layers)
        ],
        axis=0,
    ).astype(jnp.float32)
    scaled = hidden * gate
    high = scaled.astype(jnp.bfloat16)
    low = (scaled - high.astype(jnp.float32)).astype(jnp.bfloat16)
    proj = proj_ref[...]
    dims = (((1,), (1,)), ((), ()))
    result = lax.dot_general(
        high, proj, dims, preferred_element_type=jnp.float32
    ) + lax.dot_general(low, proj, dims, preferred_element_type=jnp.float32)
    rows = gate_ref.shape[3]
    order_ref[...] = jnp.concatenate(
        [
            result[((b * groups + e) * layers + l) * rows :][:rows]
            for b in range(blocks)
            for l in range(layers)
            for e in range(groups)
        ],
        axis=0,
    )
    docs, bands, _ = out_ref.shape
    step = order_ref.shape[0] // (docs * bands)
    width = order_ref.shape[1]
    for q in range(step):
        part = order_ref[pl.ds(q, docs * bands, stride=step), :]
        out_ref[:, :, q * width : (q + 1) * width] = part.reshape(docs, bands, width)


def _up_project(token_cols, weight, gate5, proj, seq):
    tokens, feats = token_cols.shape
    hidden = weight.shape[0]
    width = proj.shape[0]
    shares, layers, groups, rows = gate5.shape[:4]
    per_tile = 2
    blocks = shares // per_tile
    tile = tokens // blocks
    return pl.pallas_call(
        _up_kernel,
        grid=(blocks,),
        in_specs=[
            pl.BlockSpec((tile, feats), lambda i: (i, 0)),
            pl.BlockSpec((hidden, feats), lambda i: (0, 0)),
            pl.BlockSpec((per_tile, layers, groups, rows, hidden), lambda i: (i, 0, 0, 0, 0)),
            pl.BlockSpec((width, hidden), lambda i: (0, 0)),
        ],
        out_specs=pl.BlockSpec((tile // seq, 8, seq * width // 8), lambda i: (i, 0, 0)),
        out_shape=jax.ShapeDtypeStruct((tokens // seq, 8, seq * width // 8), jnp.float32),
        scratch_shapes=[pltpu.VMEM((tile, width), jnp.float32)],
        compiler_params=pltpu.CompilerParams(vmem_limit_bytes=48 * 1024 * 1024),
    )(token_cols, weight, gate5, proj)


def per_device(
    cotangent,
    down_weight,
    gate_act,
    layer_input,
    proj_out,
    proj_in,
    queries,
    hessian_prior,
    doc_lengths,
):
    layer_count, local_rows, model_width = cotangent.shape
    groups = lax.axis_size("example")
    shares = lax.axis_size("mp")
    col_width = model_width // groups
    pieces = jnp.stack(
        [cotangent[:, :, e * col_width : (e + 1) * col_width] for e in range(groups)]
    )
    pieces = jnp.broadcast_to(pieces[None], (shares,) + pieces.shape).reshape(
        shares * groups * layer_count, local_rows, col_width
    )
    routed = lax.all_to_all(
        pieces, ("mp", "example", "layer"), split_axis=0, concat_axis=0, tiled=True
    )
    token_cols = routed.reshape(-1, col_width)
    out_width = proj_out.shape[1]
    own_rows = layer_input.shape[1]
    gate5 = gate_act[0].reshape(shares, layer_count, groups, local_rows, gate_act.shape[2])
    out_part = _up_project(token_cols, down_weight[0], gate5, proj_out[0], own_rows)
    doc_devices = lax.axis_size(("mp", "example"))
    gathered = lax.all_to_all(
        out_part.reshape(doc_devices, 8, own_rows * out_width // 8),
        ("mp", "example"),
        split_axis=0,
        concat_axis=0,
        tiled=True,
    )
    out_rows = jnp.sum(gathered, axis=0).reshape(own_rows, out_width)
    in_rows = lax.dot_general(
        layer_input[0], proj_in[0], (((1,), (1,)), ((), ())), preferred_element_type=jnp.float32
    )
    in_width = in_rows.shape[1]
    docs_here = doc_lengths.shape[0]
    seq_len = own_rows // docs_here
    doc_scale = 1.0 / seq_len**0.5
    positions = jnp.arange(seq_len)
    valid_mask = (positions[None, :] < doc_lengths[:, None]).astype(jnp.float32)
    out_docs = out_rows.reshape(docs_here, seq_len, out_width) * valid_mask[:, :, None]
    in_docs = in_rows.reshape(docs_here, seq_len, in_width)
    projected = (
        jnp.einsum("nta,ntb->nab", out_docs, in_docs, precision=lax.Precision.HIGHEST).reshape(
            docs_here, out_width * in_width
        )
        * doc_scale
    )
    doc_width = projected.shape[1]
    all_docs = lax.all_to_all(
        jnp.broadcast_to(projected.reshape(1, 8, doc_width // 8), (doc_devices, 8, doc_width // 8)),
        ("mp", "example"),
        split_axis=0,
        concat_axis=0,
        tiled=True,
    ).reshape(doc_devices, doc_width)
    doc_total = all_docs.shape[0]
    block_rows = hessian_prior.shape[1]
    first_col = lax.axis_index(("mp", "example")) * block_rows
    col_block = lax.dynamic_slice_in_dim(all_docs, first_col, block_rows, 1)
    gram_rows = lax.dot_general(
        col_block, all_docs, (((0,), (0,)), ((), ())), precision=lax.Precision.HIGHEST
    )
    hessian = hessian_prior[0] + gram_rows / doc_total
    score_part = lax.dot_general(
        queries[0].astype(jnp.float32),
        all_docs,
        (((1,), (1,)), ((), ())),
        precision=lax.Precision.HIGHEST,
    )
    layers = lax.axis_size("layer")
    score_size = score_part.size
    scores = jnp.sum(
        lax.all_to_all(
            jnp.broadcast_to(score_part.reshape(1, 8, score_size // 8), (layers, 8, score_size // 8)),
            "layer",
            split_axis=0,
            concat_axis=0,
            tiled=True,
        ),
        axis=0,
    ).reshape(score_part.shape)
    return (hessian[None], scores)


def solution(mesh):
    in_specs = (
        P(None, ("mp", "layer", "example"), None),
        P("layer", "mp", "example"),
        P("layer", None, "mp"),
        P("layer", ("mp", "example"), None),
        P("layer", None, "mp"),
        P("layer", None, None),
        P("layer", ("mp", "example"), None),
        P("layer", ("mp", "example"), None),
        P(("mp", "example")),
    )
    out_specs = (P("layer", ("mp", "example"), None), P(("mp", "example"), None))
    return jax.shard_map(
        per_device, mesh=mesh, in_specs=in_specs, out_specs=out_specs, check_vma=False
    )
```

```python
import jax
import jax.numpy as jnp
from jax import lax
from jax.sharding import PartitionSpec as P
from jax.experimental import pallas as pl
from jax.experimental.pallas import tpu as pltpu


def _up_kernel(cot_ref, w_ref, gate_ref, proj_ref, out_ref, order_ref):
    hidden = lax.dot_general(
        cot_ref[...], w_ref[...], (((1,), (1,)), ((), ())), preferred_element_type=jnp.float32
    )
    blocks, layers, groups = gate_ref.shape[:3]
    gate = jnp.concatenate(
        [
            gate_ref[b, l, e]
            for b in range(blocks)
            for e in range(groups)
            for l in range(layers)
        ],
        axis=0,
    ).astype(jnp.float32)
    scaled = hidden * gate
    high = scaled.astype(jnp.bfloat16)
    low = (scaled - high.astype(jnp.float32)).astype(jnp.bfloat16)
    proj = proj_ref[...]
    dims = (((1,), (1,)), ((), ()))
    result = lax.dot_general(
        high, proj, dims, preferred_element_type=jnp.float32
    ) + lax.dot_general(low, proj, dims, preferred_element_type=jnp.float32)
    rows = gate_ref.shape[3]
    order_ref[...] = jnp.concatenate(
        [
            result[((b * groups + e) * layers + l) * rows :][:rows]
            for b in range(blocks)
            for l in range(layers)
            for e in range(groups)
        ],
        axis=0,
    )
    docs, bands, _ = out_ref.shape
    step = order_ref.shape[0] // (docs * bands)
    width = order_ref.shape[1]
    for q in range(step):
        part = order_ref[pl.ds(q, docs * bands, stride=step), :]
        out_ref[:, :, q * width : (q + 1) * width] = part.reshape(docs, bands, width)


def _up_project(token_cols, weight, gate5, proj, seq):
    tokens, feats = token_cols.shape
    hidden = weight.shape[0]
    width = proj.shape[0]
    shares, layers, groups, rows = gate5.shape[:4]
    per_tile = 4
    blocks = shares // per_tile
    tile = tokens // blocks
    return pl.pallas_call(
        _up_kernel,
        grid=(blocks,),
        in_specs=[
            pl.BlockSpec((tile, feats), lambda i: (i, 0)),
            pl.BlockSpec((hidden, feats), lambda i: (0, 0)),
            pl.BlockSpec((per_tile, layers, groups, rows, hidden), lambda i: (i, 0, 0, 0, 0)),
            pl.BlockSpec((width, hidden), lambda i: (0, 0)),
        ],
        out_specs=pl.BlockSpec((tile // seq, 8, seq * width // 8), lambda i: (i, 0, 0)),
        out_shape=jax.ShapeDtypeStruct((tokens // seq, 8, seq * width // 8), jnp.float32),
        scratch_shapes=[pltpu.VMEM((tile, width), jnp.float32)],
        compiler_params=pltpu.CompilerParams(vmem_limit_bytes=48 * 1024 * 1024),
    )(token_cols, weight, gate5, proj)


def per_device(
    cotangent,
    down_weight,
    gate_act,
    layer_input,
    proj_out,
    proj_in,
    queries,
    hessian_prior,
    doc_lengths,
):
    layer_count, local_rows, model_width = cotangent.shape
    groups = lax.axis_size("example")
    shares = lax.axis_size("mp")
    col_width = model_width // groups
    pieces = jnp.stack(
        [cotangent[:, :, e * col_width : (e + 1) * col_width] for e in range(groups)]
    )
    pieces = jnp.broadcast_to(pieces[None], (shares,) + pieces.shape).reshape(
        shares * groups * layer_count, local_rows, col_width
    )
    routed = lax.all_to_all(
        pieces, ("mp", "example", "layer"), split_axis=0, concat_axis=0, tiled=True
    )
    token_cols = routed.reshape(-1, col_width)
    out_width = proj_out.shape[1]
    own_rows = layer_input.shape[1]
    gate5 = gate_act[0].reshape(shares, layer_count, groups, local_rows, gate_act.shape[2])
    out_part = _up_project(token_cols, down_weight[0], gate5, proj_out[0], own_rows)
    doc_devices = lax.axis_size(("mp", "example"))
    gathered = lax.all_to_all(
        out_part.reshape(doc_devices, 8, own_rows * out_width // 8),
        ("mp", "example"),
        split_axis=0,
        concat_axis=0,
        tiled=True,
    )
    out_rows = jnp.sum(gathered, axis=0).reshape(own_rows, out_width)
    in_rows = lax.dot_general(
        layer_input[0], proj_in[0], (((1,), (1,)), ((), ())), preferred_element_type=jnp.float32
    )
    in_width = in_rows.shape[1]
    docs_here = doc_lengths.shape[0]
    seq_len = own_rows // docs_here
    doc_scale = 1.0 / seq_len**0.5
    positions = jnp.arange(seq_len)
    valid_mask = (positions[None, :] < doc_lengths[:, None]).astype(jnp.float32)
    out_docs = out_rows.reshape(docs_here, seq_len, out_width) * valid_mask[:, :, None]
    in_docs = in_rows.reshape(docs_here, seq_len, in_width)
    projected = (
        jnp.einsum("nta,ntb->nab", out_docs, in_docs, precision=lax.Precision.HIGHEST).reshape(
            docs_here, out_width * in_width
        )
        * doc_scale
    )
    doc_width = projected.shape[1]
    all_docs = lax.all_to_all(
        jnp.broadcast_to(projected.reshape(1, 8, doc_width // 8), (doc_devices, 8, doc_width // 8)),
        ("mp", "example"),
        split_axis=0,
        concat_axis=0,
        tiled=True,
    ).reshape(doc_devices, doc_width)
    doc_total = all_docs.shape[0]
    block_rows = hessian_prior.shape[1]
    first_col = lax.axis_index(("mp", "example")) * block_rows
    col_block = lax.dynamic_slice_in_dim(all_docs, first_col, block_rows, 1)
    gram_rows = lax.dot_general(
        col_block, all_docs, (((0,), (0,)), ((), ())), precision=lax.Precision.HIGHEST
    )
    hessian = hessian_prior[0] + gram_rows / doc_total
    score_part = lax.dot_general(
        queries[0].astype(jnp.float32),
        all_docs,
        (((1,), (1,)), ((), ())),
        precision=lax.Precision.HIGHEST,
    )
    layers = lax.axis_size("layer")
    score_size = score_part.size
    scores = jnp.sum(
        lax.all_to_all(
            jnp.broadcast_to(score_part.reshape(1, 8, score_size // 8), (layers, 8, score_size // 8)),
            "layer",
            split_axis=0,
            concat_axis=0,
            tiled=True,
        ),
        axis=0,
    ).reshape(score_part.shape)
    return (hessian[None], scores)


def solution(mesh):
    in_specs = (
        P(None, ("mp", "layer", "example"), None),
        P("layer", "mp", "example"),
        P("layer", None, "mp"),
        P("layer", ("mp", "example"), None),
        P("layer", None, "mp"),
        P("layer", None, None),
        P("layer", ("mp", "example"), None),
        P("layer", ("mp", "example"), None),
        P(("mp", "example")),
    )
    out_specs = (P("layer", ("mp", "example"), None), P(("mp", "example"), None))
    return jax.shard_map(
        per_device, mesh=mesh, in_specs=in_specs, out_specs=out_specs, check_vma=False
    )
```
